32 devices in a mesh: grp: 2 (over x), dev: 16 (over z, y, core).
Axes of the slice: x: 2, y: 2, z: 4, core: 2. Of those that a mesh axis runs over, the one named last changes fastest.
Arguments:
- a_blocks: bfloat16 [16384, 768], P(('grp', 'dev')), may hold values from -1.5 to 1.5
- a_cols: int32 [256, 12], P(('grp', 'dev')), may hold values from 0 to 255, as said below
- p_blocks: bfloat16 [16384, 256], P(('grp', 'dev')), may hold values from -0.375 to 0.375
- p_cols: int32 [256, 4], P(('grp', 'dev')), may hold values from 0 to 63, as said below
Outputs:
- c_coarse: bfloat16 [2, 2048, 896], P(None, 'dev')
The draws below stay inside these ranges and needn't reach their ends.
Inputs may be any that keep to these rules, and one draw needn't show every extreme that they name: a_cols[i,0] = i, and every entry of block row i lies from (i // 8 - 1) * 8 to (i // 8 + 2) * 8 - 1. p_cols[i,0] = (i // 8) * 2 + (i % 8) * 2 // 8, the aggregate of fine block row i; the entries of one row are distinct and lie from (i // 8 - 1) * 2 to (i // 8 + 2) * 2 - 1.
All inputs are finite; a program needn't handle non-finite values.
Results may differ from the reference program's by a relative error of at most 0.005.
Values may be sent and summed in bfloat16 or wider, within the bound.
No kernel may reach another device: no remote copies, remote signals or barrier semaphores. Data moves between devices by JAX's collectives and lax.ppermute only.
A program may use at most 64 MiB of HBM per device.

```python
import jax
import jax.numpy as jnp
from jax import lax

B = 64
KA = 12
KP = 4
NC = 2
RB = 8
NFB = 256
NCB = 64
N_GRP = 2
N_DEV = 16


def draw_a_cols(key, part):
    rows = jnp.arange(NFB, dtype=jnp.int32)
    base = rows // RB * RB
    offsets = jax.random.randint(key, (NFB, KA), -RB, 2 * RB, dtype=jnp.int32)
    columns = jnp.clip(base[:, None] + offsets, 0, NFB - 1)
    return jnp.concatenate([rows[:, None], columns[:, 1:]], axis=1).astype(jnp.int32)


def draw_p_cols(key, part):
    rows = jnp.arange(NFB, dtype=jnp.int32)
    device = rows // RB
    own_agg = device * NC + rows % RB * NC // RB
    offsets = jnp.arange(3 * NC, dtype=jnp.int32)
    candidate = (device[:, None] - 1) * NC + offsets[None, :]
    usable = (candidate >= 0) & (candidate < NCB) & (candidate != own_agg[:, None])
    scores = jax.random.randint(key, (NFB, 3 * NC), 0, 65536, dtype=jnp.int32) * (3 * NC) + offsets[None, :]
    scores = jnp.where(usable, scores, scores + 268435456)
    ordering = jnp.argsort(scores, axis=1, stable=True)
    chosen = jnp.take_along_axis(candidate, ordering[:, :KP - 1], axis=1)
    return jnp.concatenate([own_agg[:, None], chosen], axis=1).astype(jnp.int32)


def block_levels(rng, shape, shards, least, largest):
    def one(axis_at, blocks):
        steps = jax.random.uniform(jax.random.fold_in(jax.random.fold_in(rng, 6), axis_at), (blocks,), jnp.float32, least / len(shards), largest / len(shards))
        return jnp.repeat(jnp.exp(steps), shape[axis_at] // blocks).reshape((-1,) + (1,) * (len(shape) - axis_at - 1))

    gain = one(*shards[0])
    for cut in shards[1:]:
        gain = gain * one(*cut)
    return gain


def gaussian(rng, shape, width, limit, pieces=(), kind=jnp.bfloat16):
    values = jax.random.normal(rng, shape, jnp.float32) * width
    if len(pieces) > 0:
        values = block_levels(rng, shape, pieces, -0.22, 0.18) * values
    return jnp.clip(values, min=-limit, max=limit).astype(kind)


def setup_inputs(seed: int = 0) -> dict:
    key_of = jax.random.split(jax.random.key(seed), 5)
    return {
        "a_blocks": gaussian(key_of[0], (NFB * B, KA * B), 0.25, 1.5, ((0, 32),)),
        "a_cols": draw_a_cols(jax.random.fold_in(key_of[4], 71), 0),
        "p_blocks": gaussian(key_of[2], (NFB * B, KP * B), (4 * B) ** -0.5, 0.375, ((0, 32),)),
        "p_cols": draw_p_cols(jax.random.fold_in(key_of[4], 71), 0),
    }


def one_hot(values, levels):
    return (values[..., None] == jnp.arange(levels, dtype=jnp.int32)).astype(jnp.float32)


def device_rows(a_rows, a_cols_rows, p_near, pcol_near, device):
    local_cols = a_cols_rows - (device - 1) * RB
    picked = jnp.take(p_near, local_cols, axis=0).reshape(RB, KA, B, KP, B).astype(jnp.float32)
    target = jnp.take(pcol_near, local_cols, axis=0) - (device - 2) * NC
    column_hot = one_hot(target, 5 * NC)
    a_four = a_rows.reshape(RB, B, KA, B).astype(jnp.float32)
    blocks = jnp.einsum("irks,ikslt->irklt", a_four, picked, precision=lax.Precision.HIGHEST)
    coupled = jnp.einsum("irklt,iklj->irjt", blocks, column_hot, precision=lax.Precision.HIGHEST).astype(jnp.bfloat16)
    own_block = p_near[RB:2 * RB].reshape(RB, B, KP, B).astype(jnp.float32)
    row_hot = one_hot(pcol_near[RB:2 * RB] - (device - 1) * NC, 3 * NC)
    scattered = jnp.einsum("irms,imo->iros", own_block, row_hot, precision=lax.Precision.HIGHEST).astype(jnp.bfloat16)
    partial_value = jnp.einsum("iros,irjt->osjt", scattered.astype(jnp.float32), coupled.astype(jnp.float32), precision=lax.Precision.HIGHEST)
    return partial_value.reshape(3, NC * B, 5 * NC * B)


def reference(a_blocks, a_cols, p_blocks, p_cols):
    devices = N_GRP * N_DEV
    p_rows = p_blocks.reshape(NFB, B, KP * B)
    zero_rows = jnp.zeros((RB, B, KP * B), p_rows.dtype)
    p_padded = jnp.concatenate([zero_rows, p_rows, zero_rows], axis=0)
    zero_cols = jnp.zeros((RB, KP), jnp.int32)
    pcol_padded = jnp.concatenate([zero_cols, p_cols.astype(jnp.int32), zero_cols], axis=0)

    def one_device(device):
        start = (device * RB).astype(jnp.int32)
        a_rows = lax.dynamic_slice_in_dim(a_blocks, (start * B).astype(jnp.int32), RB * B, 0)
        a_cols_rows = lax.dynamic_slice_in_dim(a_cols, start, RB, 0)
        p_near = lax.dynamic_slice_in_dim(p_padded, start, 3 * RB, 0)
        pcol_near = lax.dynamic_slice_in_dim(pcol_padded, start, 3 * RB, 0)
        return device_rows(a_rows, a_cols_rows, p_near, pcol_near, device)

    partials = lax.map(one_device, jnp.arange(devices, dtype=jnp.int32))
    span = NC * B
    empty = jnp.zeros_like(partials[:1, 0])
    from_right = jnp.concatenate([partials[1:, 0], empty], axis=0)
    from_left = jnp.concatenate([empty, partials[:-1, 2]], axis=0)
    combined = jnp.pad(partials[:, 1], ((0, 0), (0, 0), (span, span)))
    combined = combined + jnp.pad(from_right, ((0, 0), (0, 0), (2 * span, 0)))
    combined = combined + jnp.pad(from_left, ((0, 0), (0, 0), (0, 2 * span)))
    return combined.astype(jnp.bfloat16).reshape(N_GRP, N_DEV * NC * B, 7 * NC * B)
```

```python
import jax
import jax.numpy as jnp
from jax import lax
from jax.sharding import PartitionSpec as P

B = 64
KA = 12
KP = 4
NC = 2
RB = 8
LINE = ("grp", "dev")
WIDEN = False


def mm(spec, x, y):
    if WIDEN:
        x, y = x.astype(jnp.float32), y.astype(jnp.float32)
    return jnp.einsum(spec, x, y, preferred_element_type=jnp.float32)


def shifted(x, axis, by):
    peers = lax.axis_size(axis)
    pairs = [(i, i + by) for i in range(peers) if 0 <= i + by < peers]
    return lax.ppermute(x, axis, pairs)


def partner_2(x, axis, bit):
    return lax.ppermute(x, axis, [(i, i ^ 1 << bit) for i in range(lax.axis_size(axis))])


def spread(blocks, cols, width):
    slots = jnp.arange(width, dtype=jnp.int32)[None, None, :, None]
    out = jnp.zeros(blocks.shape[:2] + (width, B), blocks.dtype)
    for l in range(KP):
        hit = cols[:, l][:, None, None, None] == slots
        out = jnp.where(hit, blocks[:, :, l : l + 1, :], out)
    return out


def local(a_blocks, a_cols, p_blocks, p_cols):
    q = lax.axis_index(LINE)
    rel = (p_cols - (q - 1) * NC).astype(jnp.bfloat16)
    tag = jnp.zeros((16, KP * B), jnp.bfloat16).at[:RB, :KP].set(rel)
    payload = jnp.concatenate([p_blocks, tag], axis=0)
    from_left = shifted(payload, LINE, 1)
    from_right = shifted(payload, LINE, -1)

    def rows(x):
        return x[: RB * B].reshape(RB, B, KP, B)

    def cols(x, shift):
        return x[RB * B : RB * B + RB, :KP].astype(jnp.int32) + shift

    p_near = jnp.concatenate([rows(from_left), rows(payload), rows(from_right)], axis=0)
    pc_near = jnp.concatenate([cols(from_left, 0), cols(payload, NC), cols(from_right, 2 * NC)], axis=0)
    ps = spread(p_near, pc_near, 5 * NC).reshape(3 * RB * B, 5 * NC * B)

    local_cols = a_cols - (q - 1) * RB
    hot = (local_cols[:, :, None] == jnp.arange(3 * RB, dtype=jnp.int32)).astype(jnp.bfloat16)
    a4 = a_blocks.reshape(RB, B, KA, B)
    dense = mm("iskt,ikr->isrt", a4, hot)
    dense = dense.reshape(RB * B, 3 * RB * B)
    hi = dense.astype(jnp.bfloat16)
    lo = (dense - hi.astype(jnp.float32)).astype(jnp.bfloat16)
    ap = mm("ar,rc->ac", hi, ps) + mm("ar,rc->ac", lo, ps)
    ap = ap.astype(jnp.bfloat16)

    own = p_blocks.reshape(RB, B, KP, B)
    scattered = spread(own, p_cols - (q - 1) * NC, 3 * NC).reshape(RB * B, 3 * NC * B)
    partial_value = mm("ro,rc->oc", scattered, ap)
    partial_value = partial_value.reshape(3, NC * B, 5 * NC * B)
    from_right_p = shifted(partial_value[0], LINE, -1)
    from_left_p = shifted(partial_value[2], LINE, 1)
    span = NC * B
    combined = jnp.pad(partial_value[1], ((0, 0), (span, span)))
    combined = combined + jnp.pad(from_right_p, ((0, 0), (2 * span, 0)))
    combined = combined + jnp.pad(from_left_p, ((0, 0), (0, 2 * span)))
    rows_here = combined.astype(jnp.bfloat16)[None]
    group = lax.axis_index("grp")
    joined = rows_here
    for section_bit in range(lax.axis_size("grp").bit_length() - 1):
        partner = partner_2(joined, "grp", section_bit)
        is_upper = group // 2**section_bit % 2 == 1
        joined = jnp.where(
            is_upper,
            jnp.concatenate([partner, joined], axis=0),
            jnp.concatenate([joined, partner], axis=0),
        )
    return joined


def solution(mesh):
    placed = (P(LINE, None),) * 4
    return jax.shard_map(
        local, mesh=mesh, in_specs=placed, out_specs=P(None, "dev", None), check_vma=False
    )
```

```python
import jax
import jax.numpy as jnp
from jax import lax
from jax.sharding import PartitionSpec as P

B = 64
KA = 12
KP = 4
NC = 2
RB = 8
LINE = ("grp", "dev")
WIDEN = False


def mm(spec, x, y):
    if WIDEN:
        x, y = x.astype(jnp.float32), y.astype(jnp.float32)
    return jnp.einsum(spec, x, y, preferred_element_type=jnp.float32)


def shifted(x, axis, by):
    peers = lax.axis_size(axis)
    pairs = [(i, i + by) for i in range(peers) if 0 <= i + by < peers]
    return lax.ppermute(x, axis, pairs)


def partner_2(x, axis, bit):
    return lax.ppermute(x, axis, [(i, i ^ 1 << bit) for i in range(lax.axis_size(axis))])


def spread2d(flat, cols, width):
    per_row = jnp.repeat(cols, B, axis=0)
    pieces = []
    for j in range(width):
        piece = jnp.zeros((flat.shape[0], B), flat.dtype)
        for l in range(KP):
            piece = jnp.where(per_row[:, l : l + 1] == j, flat[:, l * B : (l + 1) * B], piece)
        pieces.append(piece)
    return jnp.concatenate(pieces, axis=1)


def local(a_blocks, a_cols, p_blocks, p_cols):
    q = lax.axis_index(LINE)
    rel = (p_cols - (q - 1) * NC).astype(jnp.bfloat16)
    tag = jnp.zeros((16, KP * B), jnp.bfloat16).at[:RB, :KP].set(rel)
    payload = jnp.concatenate([p_blocks, tag], axis=0)
    from_left = shifted(payload, LINE, 1)
    from_right = shifted(payload, LINE, -1)

    def cols(x, shift):
        return x[RB * B : RB * B + RB, :KP].astype(jnp.int32) + shift

    p_near = jnp.concatenate([from_left[: RB * B], p_blocks, from_right[: RB * B]], axis=0)
    pc_near = jnp.concatenate([cols(from_left, 0), p_cols - (q - 2) * NC, cols(from_right, 2 * NC)], axis=0)
    ps = spread2d(p_near, pc_near, 5 * NC)

    local_cols = jnp.repeat(a_cols - (q - 1) * RB, B, axis=0)
    dense = []
    for r in range(3 * RB):
        block = jnp.zeros((RB * B, B), jnp.float32)
        for k in range(KA):
            block = block + jnp.where(
                local_cols[:, k : k + 1] == r, a_blocks[:, k * B : (k + 1) * B].astype(jnp.float32), 0.0
            )
        dense.append(block)
    dense = jnp.concatenate(dense, axis=1)
    hi = dense.astype(jnp.bfloat16)
    lo = (dense - hi.astype(jnp.float32)).astype(jnp.bfloat16)
    ap = mm("ar,rc->ac", hi, ps) + mm("ar,rc->ac", lo, ps)
    ap = ap.astype(jnp.bfloat16)

    scattered = spread2d(p_blocks, p_cols - (q - 1) * NC, 3 * NC)
    partial_value = mm("ro,rc->oc", scattered, ap)
    partial_value = partial_value.reshape(3, NC * B, 5 * NC * B)
    from_right_p = shifted(partial_value[0], LINE, -1)
    from_left_p = shifted(partial_value[2], LINE, 1)
    span = NC * B
    combined = jnp.pad(partial_value[1], ((0, 0), (span, span)))
    combined = combined + jnp.pad(from_right_p, ((0, 0), (2 * span, 0)))
    combined = combined + jnp.pad(from_left_p, ((0, 0), (0, 2 * span)))
    rows_here = combined.astype(jnp.bfloat16)[None]
    group = lax.axis_index("grp")
    joined = rows_here
    for section_bit in range(lax.axis_size("grp").bit_length() - 1):
        partner = partner_2(joined, "grp", section_bit)
        is_upper = group // 2**section_bit % 2 == 1
        joined = jnp.where(
            is_upper,
            jnp.concatenate([partner, joined], axis=0),
            jnp.concatenate([joined, partner], axis=0),
        )
    return joined


def solution(mesh):
    placed = (P(LINE, None),) * 4
    return jax.shard_map(
        local, mesh=mesh, in_specs=placed, out_specs=P(None, "dev", None), check_vma=False
    )
```

```python
import jax
import jax.numpy as jnp
from jax import lax
from jax.experimental import pallas as pl
from jax.experimental.pallas import tpu as pltpu
from jax.sharding import PartitionSpec as P

B = 64
KA = 12
KP = 4
NC = 2
RB = 8
LINE = ("grp", "dev")
HALF = 128


def shifted(x, axis, by):
    peers = lax.axis_size(axis)
    pairs = [(i, i + by) for i in range(peers) if 0 <= i + by < peers]
    return lax.ppermute(x, axis, pairs)


def partner_2(x, axis, bit):
    return lax.ppermute(x, axis, [(i, i ^ 1 << bit) for i in range(lax.axis_size(axis))])


def chunk(j):
    return pl.ds(pl.multiple_of(j * HALF, HALF), HALF)


def rows_at(r):
    return pl.ds(pl.multiple_of(r * B, B), B)


def product_kernel(lc_ref, pc_ref, po_ref, a_ref, pl_ref, pm_ref, pr_ref, out_ref, ps_ref, panel_ref, ap_ref, st_ref):
    side = lax.broadcasted_iota(jnp.int32, (B, HALF), 1) // B
    ps_ref[...] = jnp.zeros(ps_ref.shape, ps_ref.dtype)
    sources = (pl_ref, pm_ref, pr_ref)
    for r in range(3 * RB):
        blk = sources[r // RB][(r % RB) * B : (r % RB + 1) * B, :].astype(jnp.float32)
        halves = [blk[:, 0:HALF], blk[:, HALF : 2 * HALF]]
        swapped = [pltpu.roll(h, B, 1) for h in halves]
        for l in range(KP):
            j = pc_ref[r, l]
            h = j % 2
            val = jnp.where(h == l % 2, halves[l // 2], swapped[l // 2])
            cols = chunk(j // 2)
            cur = ps_ref[r * B : (r + 1) * B, cols].astype(jnp.float32)
            ps_ref[r * B : (r + 1) * B, cols] = jnp.where(side == h, val, cur).astype(ps_ref.dtype)
    for i in range(RB):
        for k in range(KA):
            panel_ref[k * B : (k + 1) * B, :] = ps_ref[rows_at(lc_ref[i, k]), :]
        ap = jnp.dot(a_ref[i * B : (i + 1) * B, :], panel_ref[...], preferred_element_type=jnp.float32)
        ap_ref[i * B : (i + 1) * B, :] = ap.astype(ap_ref.dtype)
    pt = pm_ref[...].astype(jnp.float32).T
    st_ref[...] = jnp.zeros(st_ref.shape, st_ref.dtype)
    for i in range(RB):
        cols = slice((i // 2) * HALF, (i // 2 + 1) * HALF)
        for l in range(KP):
            dest = rows_at(po_ref[i, l])
            cur = st_ref[dest, cols]
            st_ref[dest, cols] = jnp.where(side == i % 2, pt[l * B : (l + 1) * B, cols], cur)
    out_ref[...] = jnp.dot(
        st_ref[...].astype(jnp.bfloat16), ap_ref[...], preferred_element_type=jnp.float32
    )


def products(lc, pc, po, a_blocks, left, own, right):
    smem = pl.BlockSpec(memory_space=pltpu.SMEM)
    vmem = pl.BlockSpec(memory_space=pltpu.VMEM)
    near = 3 * RB * B
    return pl.pallas_call(
        product_kernel,
        out_shape=jax.ShapeDtypeStruct((3 * NC * B, 5 * NC * B), jnp.float32),
        in_specs=[smem] * 3 + [vmem] * 4,
        out_specs=vmem,
        scratch_shapes=[
            pltpu.VMEM((near, 5 * NC * B), jnp.bfloat16),
            pltpu.VMEM((KA * B, 5 * NC * B), jnp.bfloat16),
            pltpu.VMEM((RB * B, 5 * NC * B), jnp.bfloat16),
            pltpu.VMEM((3 * NC * B, RB * B), jnp.float32),
        ],
        cost_estimate=pl.CostEstimate(
            flops=2 * RB * B * KA * B * 5 * NC * B + 2 * 3 * NC * B * RB * B * 5 * NC * B,
            bytes_accessed=4 * 1024 * 1024,
            transcendentals=0,
        ),
    )(lc, pc, po, a_blocks, left, own, right)


def local(a_blocks, a_cols, p_blocks, p_cols):
    q = lax.axis_index(LINE)
    rel = (p_cols - (q - 1) * NC).astype(jnp.bfloat16)
    tag = jnp.zeros((16, KP * B), jnp.bfloat16).at[:RB, :KP].set(rel)
    payload = jnp.concatenate([p_blocks, tag], axis=0)
    from_left = shifted(payload, LINE, 1)
    from_right = shifted(payload, LINE, -1)

    def cols(x, shift):
        return x[RB * B : RB * B + RB, :KP].astype(jnp.int32) + shift

    pc = jnp.concatenate([cols(from_left, 0), p_cols - (q - 2) * NC, cols(from_right, 2 * NC)], axis=0)
    lc = a_cols - (q - 1) * RB
    po = p_cols - (q - 1) * NC
    partial_value = products(lc, pc, po, a_blocks, from_left, p_blocks, from_right)

    partial_value = partial_value.reshape(3, NC * B, 5 * NC * B)
    from_right_p = shifted(partial_value[0], LINE, -1)
    from_left_p = shifted(partial_value[2], LINE, 1)
    span = NC * B
    combined = jnp.pad(partial_value[1], ((0, 0), (span, span)))
    combined = combined + jnp.pad(from_right_p, ((0, 0), (2 * span, 0)))
    combined = combined + jnp.pad(from_left_p, ((0, 0), (0, 2 * span)))
    rows_here = combined.astype(jnp.bfloat16)[None]
    group = lax.axis_index("grp")
    joined = rows_here
    for section_bit in range(lax.axis_size("grp").bit_length() - 1):
        partner = partner_2(joined, "grp", section_bit)
        is_upper = group // 2**section_bit % 2 == 1
        joined = jnp.where(
            is_upper,
            jnp.concatenate([partner, joined], axis=0),
            jnp.concatenate([joined, partner], axis=0),
        )
    return joined


def solution(mesh):
    placed = (P(LINE, None),) * 4
    return jax.shard_map(
        local, mesh=mesh, in_specs=placed, out_specs=P(None, "dev", None), check_vma=False
    )
```

```python
import jax
import jax.numpy as jnp
from jax import lax
from jax.experimental import pallas as pl
from jax.experimental.pallas import tpu as pltpu
from jax.sharding import PartitionSpec as P

B = 64
KA = 12
KP = 4
NC = 2
RB = 8
LINE = ("grp", "dev")
HALF = 128


def shifted(x, axis, by):
    peers = lax.axis_size(axis)
    pairs = [(i, i + by) for i in range(peers) if 0 <= i + by < peers]
    return lax.ppermute(x, axis, pairs)


def partner_2(x, axis, bit):
    return lax.ppermute(x, axis, [(i, i ^ 1 << bit) for i in range(lax.axis_size(axis))])


def chunk(j):
    return pl.ds(pl.multiple_of(j * HALF, HALF), HALF)


def rows_at(r):
    return pl.ds(pl.multiple_of(r * B, B), B)


def product_kernel(lc_ref, pc_ref, po_ref, a_ref, pl_ref, pm_ref, pr_ref, out_ref, ps_ref, panel_ref, ap_ref, st_ref):
    side = lax.broadcasted_iota(jnp.int32, (B, HALF), 1) // B
    ps_ref[...] = jnp.zeros(ps_ref.shape, ps_ref.dtype)
    sources = (pl_ref, pm_ref, pr_ref)
    for r in range(3 * RB):
        blk = sources[r // RB][(r % RB) * B : (r % RB + 1) * B, :].astype(jnp.float32)
        halves = [blk[:, 0:HALF], blk[:, HALF : 2 * HALF]]
        swapped = [pltpu.roll(h, B, 1) for h in halves]
        for l in range(KP):
            j = pc_ref[r, l]
            h = j % 2
            val = jnp.where(h == l % 2, halves[l // 2], swapped[l // 2])
            cols = chunk(j // 2)
            cur = ps_ref[r * B : (r + 1) * B, cols].astype(jnp.float32)
            ps_ref[r * B : (r + 1) * B, cols] = jnp.where(side == h, val, cur).astype(ps_ref.dtype)
    for i in range(RB):
        for k in range(KA):
            panel_ref[k * B : (k + 1) * B, :] = ps_ref[rows_at(lc_ref[i, k]), :]
        ap = jnp.dot(a_ref[i * B : (i + 1) * B, :], panel_ref[...], preferred_element_type=jnp.float32)
        ap_ref[i * B : (i + 1) * B, :] = ap.astype(ap_ref.dtype)
    pt = pm_ref[...].astype(jnp.float32).T
    st_ref[...] = jnp.zeros(st_ref.shape, st_ref.dtype)
    for i in range(RB):
        cols = slice((i // 2) * HALF, (i // 2 + 1) * HALF)
        for l in range(KP):
            dest = rows_at(po_ref[i, l])
            cur = st_ref[dest, cols]
            st_ref[dest, cols] = jnp.where(side == i % 2, pt[l * B : (l + 1) * B, cols], cur)
    out_ref[...] = jnp.dot(
        st_ref[...].astype(jnp.bfloat16), ap_ref[...], preferred_element_type=jnp.float32
    )


def products(lc, pc, po, a_blocks, left, own, right):
    smem = pl.BlockSpec(memory_space=pltpu.SMEM)
    vmem = pl.BlockSpec(memory_space=pltpu.VMEM)
    near = 3 * RB * B
    return pl.pallas_call(
        product_kernel,
        out_shape=jax.ShapeDtypeStruct((3 * NC * B, 5 * NC * B), jnp.float32),
        in_specs=[smem] * 3 + [vmem] * 4,
        out_specs=vmem,
        scratch_shapes=[
            pltpu.VMEM((near, 5 * NC * B), jnp.bfloat16),
            pltpu.VMEM((KA * B, 5 * NC * B), jnp.bfloat16),
            pltpu.VMEM((RB * B, 5 * NC * B), jnp.bfloat16),
            pltpu.VMEM((3 * NC * B, RB * B), jnp.float32),
        ],
        cost_estimate=pl.CostEstimate(
            flops=2 * RB * B * KA * B * 5 * NC * B + 2 * 3 * NC * B * RB * B * 5 * NC * B,
            bytes_accessed=4 * 1024 * 1024,
            transcendentals=0,
        ),
    )(lc, pc, po, a_blocks, left, own, right)


def local(a_blocks, a_cols, p_blocks, p_cols):
    q = lax.axis_index(LINE)
    rel = (p_cols - (q - 1) * NC).astype(jnp.bfloat16)
    tag = jnp.zeros((16, KP * B), jnp.bfloat16).at[:RB, :KP].set(rel)
    payload = jnp.concatenate([p_blocks, tag], axis=0)
    from_left = shifted(payload, LINE, 1)
    from_right = shifted(payload, LINE, -1)

    def cols(x, shift):
        return x[RB * B : RB * B + RB, :KP].astype(jnp.int32) + shift

    pc = jnp.concatenate([cols(from_left, 0), p_cols - (q - 2) * NC, cols(from_right, 2 * NC)], axis=0)
    lc = a_cols - (q - 1) * RB
    po = p_cols - (q - 1) * NC
    partial_value = products(lc, pc, po, a_blocks, from_left, p_blocks, from_right)

    partial_value = partial_value.reshape(3, NC * B, 5 * NC * B)
    n_grp, n_dev = lax.axis_size("grp"), lax.axis_size("dev")
    n = n_grp * n_dev
    group = lax.axis_index("grp")

    def moved(x, rows_of):
        outs = []
        for delta in range(n_grp):
            pairs = []
            for src in range(n):
                dst = rows_of(src)
                if 0 <= dst < n:
                    pairs.append((src, (dst // n_dev + delta) % n_grp * n_dev + dst % n_dev))
            outs.append(lax.ppermute(x, LINE, pairs) if pairs != [(i, i) for i in range(n)] else x)
        return outs

    own = moved(partial_value[1], lambda src: src)
    from_next = moved(partial_value[0], lambda src: src - 1)
    from_prev = moved(partial_value[2], lambda src: src + 1)
    span = NC * B
    stacked = []
    for delta in range(n_grp):
        combined = jnp.pad(own[delta], ((0, 0), (span, span)))
        combined = combined + jnp.pad(from_next[delta], ((0, 0), (2 * span, 0)))
        combined = combined + jnp.pad(from_prev[delta], ((0, 0), (0, 2 * span)))
        stacked.append(combined.astype(jnp.bfloat16))
    stacked = jnp.stack(stacked)
    order = (group - jnp.arange(n_grp, dtype=jnp.int32)) % n_grp
    return jnp.take(stacked, order, axis=0)


def solution(mesh):
    placed = (P(LINE, None),) * 4
    return jax.shard_map(
        local, mesh=mesh, in_specs=placed, out_specs=P(None, "dev", None), check_vma=False
    )
```

```python
import jax
import jax.numpy as jnp
from jax import lax
from jax.experimental import pallas as pl
from jax.experimental.pallas import tpu as pltpu
from jax.sharding import PartitionSpec as P

B = 64
KA = 12
KP = 4
NC = 2
RB = 8
LINE = ("grp", "dev")
HALF = 128


def shifted(x, axis, by):
    peers = lax.axis_size(axis)
    pairs = [(i, i + by) for i in range(peers) if 0 <= i + by < peers]
    return lax.ppermute(x, axis, pairs)


def partner_2(x, axis, bit):
    return lax.ppermute(x, axis, [(i, i ^ 1 << bit) for i in range(lax.axis_size(axis))])


def chunk(j):
    return pl.ds(pl.multiple_of(j * HALF, HALF), HALF)


def rows_at(r):
    return pl.ds(pl.multiple_of(r * B, B), B)


def product_kernel(
    lc_ref, pc_ref, po_ref, a_ref, pl_ref, pm_ref, pr_ref, prev_ref, here_ref, next_ref, ps_ref, panel_ref, ap_ref, st_ref
):
    side = lax.broadcasted_iota(jnp.int32, (B, HALF), 1) // B
    ps_ref[...] = jnp.zeros(ps_ref.shape, ps_ref.dtype)
    sources = (pl_ref, pm_ref, pr_ref)
    for r in range(3 * RB):
        blk = sources[r // RB][(r % RB) * B : (r % RB + 1) * B, :].astype(jnp.float32)
        halves = [blk[:, 0:HALF], blk[:, HALF : 2 * HALF]]
        swapped = [pltpu.roll(h, B, 1) for h in halves]
        for l in range(KP):
            j = pc_ref[r, l]
            h = j % 2
            val = jnp.where(h == l % 2, halves[l // 2], swapped[l // 2])
            cols = chunk(j // 2)
            cur = ps_ref[r * B : (r + 1) * B, cols].astype(jnp.float32)
            ps_ref[r * B : (r + 1) * B, cols] = jnp.where(side == h, val, cur).astype(ps_ref.dtype)
    for i in range(RB):
        for k in range(KA):
            panel_ref[k * B : (k + 1) * B, :] = ps_ref[rows_at(lc_ref[i, k]), :]
        ap = jnp.dot(a_ref[i * B : (i + 1) * B, :], panel_ref[...], preferred_element_type=jnp.float32)
        ap_ref[i * B : (i + 1) * B, :] = ap.astype(ap_ref.dtype)
    pt = pm_ref[...].astype(jnp.float32).T
    st_ref[...] = jnp.zeros(st_ref.shape, st_ref.dtype)
    for i in range(RB):
        cols = slice((i // 2) * HALF, (i // 2 + 1) * HALF)
        for l in range(KP):
            dest = rows_at(po_ref[i, l])
            cur = st_ref[dest, cols]
            st_ref[dest, cols] = jnp.where(side == i % 2, pt[l * B : (l + 1) * B, cols], cur)
    span = NC * B
    for o, out_ref in enumerate((prev_ref, here_ref, next_ref)):
        out_ref[...] = jnp.dot(
            st_ref[o * span : (o + 1) * span, :].astype(jnp.bfloat16),
            ap_ref[...],
            preferred_element_type=jnp.float32,
        )


def products(lc, pc, po, a_blocks, left, own, right):
    smem = pl.BlockSpec(memory_space=pltpu.SMEM)
    vmem = pl.BlockSpec(memory_space=pltpu.VMEM)
    near = 3 * RB * B
    return pl.pallas_call(
        product_kernel,
        out_shape=[jax.ShapeDtypeStruct((NC * B, 5 * NC * B), jnp.float32)] * 3,
        in_specs=[smem] * 3 + [vmem] * 4,
        out_specs=[vmem] * 3,
        scratch_shapes=[
            pltpu.VMEM((near, 5 * NC * B), jnp.bfloat16),
            pltpu.VMEM((KA * B, 5 * NC * B), jnp.bfloat16),
            pltpu.VMEM((RB * B, 5 * NC * B), jnp.bfloat16),
            pltpu.VMEM((3 * NC * B, RB * B), jnp.float32),
        ],
        cost_estimate=pl.CostEstimate(
            flops=2 * RB * B * KA * B * 5 * NC * B + 2 * 3 * NC * B * RB * B * 5 * NC * B,
            bytes_accessed=4 * 1024 * 1024,
            transcendentals=0,
        ),
    )(lc, pc, po, a_blocks, left, own, right)


def local(a_blocks, a_cols, p_blocks, p_cols):
    q = lax.axis_index(LINE)
    from_left = shifted(p_blocks, LINE, 1)
    from_right = shifted(p_blocks, LINE, -1)
    rel = p_cols - (q - 1) * NC
    cols_left = shifted(rel, LINE, 1)
    cols_right = shifted(rel, LINE, -1)
    pc = jnp.concatenate([cols_left, rel + NC, cols_right + 2 * NC], axis=0)
    lc = a_cols - (q - 1) * RB
    prev_rows, here_rows, next_rows = products(lc, pc, rel, a_blocks, from_left, p_blocks, from_right)
    from_right_p = shifted(prev_rows, LINE, -1)
    from_left_p = shifted(next_rows, LINE, 1)
    span = NC * B
    combined = jnp.pad(here_rows, ((0, 0), (span, span)))
    combined = combined + jnp.pad(from_right_p, ((0, 0), (2 * span, 0)))
    combined = combined + jnp.pad(from_left_p, ((0, 0), (0, 2 * span)))
    rows_here = combined.astype(jnp.bfloat16)[None]
    group = lax.axis_index("grp")
    joined = rows_here
    for section_bit in range(lax.axis_size("grp").bit_length() - 1):
        partner = partner_2(joined, "grp", section_bit)
        is_upper = group // 2**section_bit % 2 == 1
        joined = jnp.where(
            is_upper,
            jnp.concatenate([partner, joined], axis=0),
            jnp.concatenate([joined, partner], axis=0),
        )
    return joined


def solution(mesh):
    placed = (P(LINE, None),) * 4
    return jax.shard_map(
        local, mesh=mesh, in_specs=placed, out_specs=P(None, "dev", None), check_vma=False
    )
```

```python
import jax
import jax.numpy as jnp
from jax import lax
from jax.experimental import pallas as pl
from jax.experimental.pallas import tpu as pltpu
from jax.sharding import PartitionSpec as P

B = 64
KA = 12
KP = 4
NC = 2
RB = 8
LINE = ("grp", "dev")
HALF = 128


def shifted(x, axis, by):
    peers = lax.axis_size(axis)
    pairs = [(i, i + by) for i in range(peers) if 0 <= i + by < peers]
    return lax.ppermute(x, axis, pairs)


def partner_2(x, axis, bit):
    return lax.ppermute(x, axis, [(i, i ^ 1 << bit) for i in range(lax.axis_size(axis))])


def chunk(j):
    return pl.ds(pl.multiple_of(j * HALF, HALF), HALF)


def rows_at(r):
    return pl.ds(pl.multiple_of(r * B, B), B)


def product_kernel(
    lc_ref, pc_ref, po_ref, a_ref, pl_ref, pm_ref, pr_ref, prev_ref, here_ref, next_ref, ps_ref, panel_ref, ap_ref, st_ref
):
    side = lax.broadcasted_iota(jnp.int32, (B, HALF), 1) // B
    ps_ref[...] = jnp.zeros(ps_ref.shape, ps_ref.dtype)
    sources = (pl_ref, pm_ref, pr_ref)
    for r in range(3 * RB):
        blk = sources[r // RB][(r % RB) * B : (r % RB + 1) * B, :].astype(jnp.float32)
        halves = [blk[:, 0:HALF], blk[:, HALF : 2 * HALF]]
        swapped = [pltpu.roll(h, B, 1) for h in halves]
        for l in range(KP):
            j = pc_ref[r, l]
            h = j % 2
            val = jnp.where(h == l % 2, halves[l // 2], swapped[l // 2])
            cols = chunk(j // 2)
            cur = ps_ref[r * B : (r + 1) * B, cols].astype(jnp.float32)
            ps_ref[r * B : (r + 1) * B, cols] = jnp.where(side == h, val, cur).astype(ps_ref.dtype)
    for i in range(RB):
        for k in range(KA):
            panel_ref[k * B : (k + 1) * B, :] = ps_ref[rows_at(lc_ref[i, k]), :]
        ap = jnp.dot(a_ref[i * B : (i + 1) * B, :], panel_ref[...], preferred_element_type=jnp.float32)
        ap_ref[i * B : (i + 1) * B, :] = ap.astype(ap_ref.dtype)
    pt = pm_ref[...].astype(jnp.float32).T
    st_ref[...] = jnp.zeros(st_ref.shape, st_ref.dtype)
    for i in range(RB):
        cols = slice((i // 2) * HALF, (i // 2 + 1) * HALF)
        for l in range(KP):
            dest = rows_at(po_ref[i, l])
            cur = st_ref[dest, cols]
            st_ref[dest, cols] = jnp.where(side == i % 2, pt[l * B : (l + 1) * B, cols], cur)
    span = NC * B
    for o, out_ref in enumerate((prev_ref, here_ref, next_ref)):
        out_ref[...] = jnp.dot(
            st_ref[o * span : (o + 1) * span, :].astype(jnp.bfloat16),
            ap_ref[...],
            preferred_element_type=jnp.float32,
        )


def products(lc, pc, po, a_blocks, left, own, right):
    smem = pl.BlockSpec(memory_space=pltpu.SMEM)
    vmem = pl.BlockSpec(memory_space=pltpu.VMEM)
    near = 3 * RB * B
    return pl.pallas_call(
        product_kernel,
        out_shape=[jax.ShapeDtypeStruct((NC * B, 5 * NC * B), jnp.float32)] * 3,
        in_specs=[smem] * 3 + [vmem] * 4,
        out_specs=[vmem] * 3,
        scratch_shapes=[
            pltpu.VMEM((near, 5 * NC * B), jnp.bfloat16),
            pltpu.VMEM((KA * B, 5 * NC * B), jnp.bfloat16),
            pltpu.VMEM((RB * B, 5 * NC * B), jnp.bfloat16),
            pltpu.VMEM((3 * NC * B, RB * B), jnp.float32),
        ],
        cost_estimate=pl.CostEstimate(
            flops=2 * RB * B * KA * B * 5 * NC * B + 2 * 3 * NC * B * RB * B * 5 * NC * B,
            bytes_accessed=4 * 1024 * 1024,
            transcendentals=0,
        ),
    )(lc, pc, po, a_blocks, left, own, right)


def local(a_blocks, a_cols, p_blocks, p_cols):
    q = lax.axis_index(LINE)
    rel = p_cols - (q - 1) * NC
    tag = jnp.zeros((16, KP * B), jnp.bfloat16).at[:RB, :KP].set(rel.astype(jnp.bfloat16))
    payload = jnp.concatenate([p_blocks, tag], axis=0)
    from_left = shifted(payload, LINE, 1)
    from_right = shifted(payload, LINE, -1)

    def cols(x, shift):
        return x[RB * B : RB * B + RB, :KP].astype(jnp.int32) + shift

    pc = jnp.concatenate([cols(from_left, 0), rel + NC, cols(from_right, 2 * NC)], axis=0)
    lc = a_cols - (q - 1) * RB
    prev_rows, here_rows, next_rows = products(lc, pc, rel, a_blocks, from_left, p_blocks, from_right)
    from_right_p = shifted(prev_rows, LINE, -1)
    from_left_p = shifted(next_rows, LINE, 1)
    span = NC * B
    combined = jnp.pad(here_rows, ((0, 0), (span, span)))
    combined = combined + jnp.pad(from_right_p, ((0, 0), (2 * span, 0)))
    combined = combined + jnp.pad(from_left_p, ((0, 0), (0, 2 * span)))
    rows_here = combined.astype(jnp.bfloat16)[None]
    group = lax.axis_index("grp")
    joined = rows_here
    for section_bit in range(lax.axis_size("grp").bit_length() - 1):
        partner = partner_2(joined, "grp", section_bit)
        is_upper = group // 2**section_bit % 2 == 1
        joined = jnp.where(
            is_upper,
            jnp.concatenate([partner, joined], axis=0),
            jnp.concatenate([joined, partner], axis=0),
        )
    return joined


def solution(mesh):
    placed = (P(LINE, None),) * 4
    return jax.shard_map(
        local, mesh=mesh, in_specs=placed, out_specs=P(None, "dev", None), check_vma=False
    )
```

```python
import jax
import jax.numpy as jnp
from jax import lax
from jax.experimental import pallas as pl
from jax.experimental.pallas import tpu as pltpu
from jax.sharding import PartitionSpec as P

B = 64
KA = 12
KP = 4
NC = 2
RB = 8
LINE = ("grp", "dev")
HALF = 128


def shifted(x, axis, by):
    peers = lax.axis_size(axis)
    pairs = [(i, i + by) for i in range(peers) if 0 <= i + by < peers]
    return lax.ppermute(x, axis, pairs)


def partner_2(x, axis, bit):
    return lax.ppermute(x, axis, [(i, i ^ 1 << bit) for i in range(lax.axis_size(axis))])


def chunk(j):
    return pl.ds(pl.multiple_of(j * HALF, HALF), HALF)


def rows_at(r):
    return pl.ds(pl.multiple_of(r * B, B), B)


def product_kernel(
    lc_ref, pc_ref, po_ref, a_ref, pl_ref, pm_ref, pr_ref, prev_ref, here_ref, next_ref, ps_ref, panel_ref, ap_ref, st_ref
):
    side = lax.broadcasted_iota(jnp.int32, (B, HALF), 1) // B
    ps_ref[...] = jnp.zeros(ps_ref.shape, ps_ref.dtype)
    sources = (pl_ref, pm_ref, pr_ref)
    for r in range(3 * RB):
        blk = sources[r // RB][(r % RB) * B : (r % RB + 1) * B, :].astype(jnp.float32)
        halves = [blk[:, 0:HALF], blk[:, HALF : 2 * HALF]]
        swapped = [pltpu.roll(h, B, 1) for h in halves]
        for l in range(KP):
            j = pc_ref[r, l]
            h = j % 2
            val = jnp.where(h == l % 2, halves[l // 2], swapped[l // 2])
            cols = chunk(j // 2)
            cur = ps_ref[r * B : (r + 1) * B, cols].astype(jnp.float32)
            ps_ref[r * B : (r + 1) * B, cols] = jnp.where(side == h, val, cur).astype(ps_ref.dtype)
    for i in range(RB):
        for k in range(KA):
            panel_ref[k * B : (k + 1) * B, :] = ps_ref[rows_at(lc_ref[i, k]), :]
        ap = jnp.dot(a_ref[i * B : (i + 1) * B, :], panel_ref[...], preferred_element_type=jnp.float32)
        ap_ref[i * B : (i + 1) * B, :] = ap.astype(ap_ref.dtype)
    pt = pm_ref[...].astype(jnp.float32).T
    st_ref[...] = jnp.zeros(st_ref.shape, st_ref.dtype)
    for i in range(RB):
        cols = slice((i // 2) * HALF, (i // 2 + 1) * HALF)
        for l in range(KP):
            dest = rows_at(po_ref[i, l])
            cur = st_ref[dest, cols]
            st_ref[dest, cols] = jnp.where(side == i % 2, pt[l * B : (l + 1) * B, cols], cur)
    span = NC * B
    for o, out_ref in enumerate((prev_ref, here_ref, next_ref)):
        out_ref[...] = jnp.dot(
            st_ref[o * span : (o + 1) * span, :].astype(jnp.bfloat16),
            ap_ref[...],
            preferred_element_type=jnp.float32,
        ).astype(out_ref.dtype)


def products(lc, pc, po, a_blocks, left, own, right):
    smem = pl.BlockSpec(memory_space=pltpu.SMEM)
    vmem = pl.BlockSpec(memory_space=pltpu.VMEM)
    near = 3 * RB * B
    return pl.pallas_call(
        product_kernel,
        out_shape=[
            jax.ShapeDtypeStruct((NC * B, 5 * NC * B), dtype)
            for dtype in (jnp.bfloat16, jnp.float32, jnp.bfloat16)
        ],
        in_specs=[smem] * 3 + [vmem] * 4,
        out_specs=[vmem] * 3,
        scratch_shapes=[
            pltpu.VMEM((near, 5 * NC * B), jnp.bfloat16),
            pltpu.VMEM((KA * B, 5 * NC * B), jnp.bfloat16),
            pltpu.VMEM((RB * B, 5 * NC * B), jnp.bfloat16),
            pltpu.VMEM((3 * NC * B, RB * B), jnp.float32),
        ],
        cost_estimate=pl.CostEstimate(
            flops=2 * RB * B * KA * B * 5 * NC * B + 2 * 3 * NC * B * RB * B * 5 * NC * B,
            bytes_accessed=4 * 1024 * 1024,
            transcendentals=0,
        ),
    )(lc, pc, po, a_blocks, left, own, right)


def local(a_blocks, a_cols, p_blocks, p_cols):
    q = lax.axis_index(LINE)
    rel = p_cols - (q - 1) * NC
    tag = jnp.zeros((16, KP * B), jnp.bfloat16).at[:RB, :KP].set(rel.astype(jnp.bfloat16))
    payload = jnp.concatenate([p_blocks, tag], axis=0)
    from_left = shifted(payload, LINE, 1)
    from_right = shifted(payload, LINE, -1)

    def cols(x, shift):
        return x[RB * B : RB * B + RB, :KP].astype(jnp.int32) + shift

    pc = jnp.concatenate([cols(from_left, 0), rel + NC, cols(from_right, 2 * NC)], axis=0)
    lc = a_cols - (q - 1) * RB
    prev_rows, here_rows, next_rows = products(lc, pc, rel, a_blocks, from_left, p_blocks, from_right)
    from_right_p = shifted(prev_rows, LINE, -1)
    from_left_p = shifted(next_rows, LINE, 1)
    span = NC * B
    combined = jnp.pad(here_rows, ((0, 0), (span, span)))
    combined = combined + jnp.pad(from_right_p.astype(jnp.float32), ((0, 0), (2 * span, 0)))
    combined = combined + jnp.pad(from_left_p.astype(jnp.float32), ((0, 0), (0, 2 * span)))
    rows_here = combined.astype(jnp.bfloat16)[None]
    group = lax.axis_index("grp")
    joined = rows_here
    for section_bit in range(lax.axis_size("grp").bit_length() - 1):
        partner = partner_2(joined, "grp", section_bit)
        is_upper = group // 2**section_bit % 2 == 1
        joined = jnp.where(
            is_upper,
            jnp.concatenate([partner, joined], axis=0),
            jnp.concatenate([joined, partner], axis=0),
        )
    return joined


def solution(mesh):
    placed = (P(LINE, None),) * 4
    return jax.shard_map(
        local, mesh=mesh, in_specs=placed, out_specs=P(None, "dev", None), check_vma=False
    )
```

```python
import jax
import jax.numpy as jnp
from jax import lax
from jax.experimental import pallas as pl
from jax.experimental.pallas import tpu as pltpu
from jax.sharding import PartitionSpec as P

B = 64
KA = 12
KP = 4
NC = 2
RB = 8
LINE = ("grp", "dev")
HALF = 128


def shifted(x, axis, by):
    peers = lax.axis_size(axis)
    pairs = [(i, i + by) for i in range(peers) if 0 <= i + by < peers]
    return lax.ppermute(x, axis, pairs)


def partner_2(x, axis, bit):
    return lax.ppermute(x, axis, [(i, i ^ 1 << bit) for i in range(lax.axis_size(axis))])


def chunk(j):
    return pl.ds(pl.multiple_of(j * HALF, HALF), HALF)


def rows_at(r):
    return pl.ds(pl.multiple_of(r * B, B), B)


def spread_rows(ps_ref, base, src_ref, pc_ref, pc_base, side):
    for r in range(RB):
        blk = src_ref[r * B : (r + 1) * B, :].astype(jnp.float32)
        halves = [blk[:, 0:HALF], blk[:, HALF : 2 * HALF]]
        swapped = [pltpu.roll(h, B, 1) for h in halves]
        rows = slice((base + r) * B, (base + r + 1) * B)
        for l in range(KP):
            j = pc_ref[pc_base + r, l]
            h = j % 2
            val = jnp.where(h == l % 2, halves[l // 2], swapped[l // 2])
            cols = chunk(j // 2)
            cur = ps_ref[rows, cols].astype(jnp.float32)
            ps_ref[rows, cols] = jnp.where(side == h, val, cur).astype(ps_ref.dtype)


def own_kernel(po_ref, pm_ref, pso_ref, st_ref):
    side = lax.broadcasted_iota(jnp.int32, (B, HALF), 1) // B
    pso_ref[...] = jnp.zeros(pso_ref.shape, pso_ref.dtype)
    spread_rows(pso_ref, 0, pm_ref, po_ref, 0, side)
    pt = pm_ref[...].astype(jnp.float32).T
    st_ref[...] = jnp.zeros(st_ref.shape, st_ref.dtype)
    for i in range(RB):
        cols = slice((i // 2) * HALF, (i // 2 + 1) * HALF)
        for l in range(KP):
            dest = rows_at(po_ref[RB + i, l])
            cur = st_ref[dest, cols].astype(jnp.float32)
            st_ref[dest, cols] = jnp.where(side == i % 2, pt[l * B : (l + 1) * B, cols], cur).astype(st_ref.dtype)


def product_kernel(
    lc_ref, pc_ref, a_ref, pl_ref, pr_ref, pso_ref, st_ref, prev_ref, here_ref, next_ref, ps_ref, panel_ref, ap_ref
):
    side = lax.broadcasted_iota(jnp.int32, (B, HALF), 1) // B
    near = RB * B
    ps_ref[0:near, :] = jnp.zeros((near, ps_ref.shape[1]), ps_ref.dtype)
    ps_ref[2 * near : 3 * near, :] = jnp.zeros((near, ps_ref.shape[1]), ps_ref.dtype)
    ps_ref[near : 2 * near, :] = pso_ref[...]
    spread_rows(ps_ref, 0, pl_ref, pc_ref, 0, side)
    spread_rows(ps_ref, 2 * RB, pr_ref, pc_ref, RB, side)
    for i in range(RB):
        for k in range(KA):
            panel_ref[k * B : (k + 1) * B, :] = ps_ref[rows_at(lc_ref[i, k]), :]
        ap = jnp.dot(a_ref[i * B : (i + 1) * B, :], panel_ref[...], preferred_element_type=jnp.float32)
        ap_ref[i * B : (i + 1) * B, :] = ap.astype(ap_ref.dtype)
    span = NC * B
    for o, out_ref in enumerate((prev_ref, here_ref, next_ref)):
        out_ref[...] = jnp.dot(
            st_ref[o * span : (o + 1) * span, :], ap_ref[...], preferred_element_type=jnp.float32
        )


def products(lc, pc_side, po, a_blocks, left, own, right):
    smem = pl.BlockSpec(memory_space=pltpu.SMEM)
    vmem = pl.BlockSpec(memory_space=pltpu.VMEM)
    window = 5 * NC * B
    pso, st = pl.pallas_call(
        own_kernel,
        out_shape=[
            jax.ShapeDtypeStruct((RB * B, window), jnp.bfloat16),
            jax.ShapeDtypeStruct((3 * NC * B, RB * B), jnp.bfloat16),
        ],
        in_specs=[smem, vmem],
        out_specs=[vmem] * 2,
    )(po, own)
    return pl.pallas_call(
        product_kernel,
        out_shape=[jax.ShapeDtypeStruct((NC * B, window), jnp.float32)] * 3,
        in_specs=[smem] * 2 + [vmem] * 5,
        out_specs=[vmem] * 3,
        scratch_shapes=[
            pltpu.VMEM((3 * RB * B, window), jnp.bfloat16),
            pltpu.VMEM((KA * B, window), jnp.bfloat16),
            pltpu.VMEM((RB * B, window), jnp.bfloat16),
        ],
        cost_estimate=pl.CostEstimate(
            flops=2 * RB * B * KA * B * window + 2 * 3 * NC * B * RB * B * window,
            bytes_accessed=4 * 1024 * 1024,
            transcendentals=0,
        ),
    )(lc, pc_side, a_blocks, left, right, pso, st)


def local(a_blocks, a_cols, p_blocks, p_cols):
    q = lax.axis_index(LINE)
    rel = p_cols - (q - 1) * NC
    tag = jnp.zeros((16, KP * B), jnp.bfloat16).at[:RB, :KP].set(rel.astype(jnp.bfloat16))
    payload = jnp.concatenate([p_blocks, tag], axis=0)
    from_left = shifted(payload, LINE, 1)
    from_right = shifted(payload, LINE, -1)

    def cols(x, shift):
        return x[RB * B : RB * B + RB, :KP].astype(jnp.int32) + shift

    pc_side = jnp.concatenate([cols(from_left, 0), cols(from_right, 2 * NC)], axis=0)
    po = jnp.concatenate([rel + NC, rel], axis=0)
    lc = a_cols - (q - 1) * RB
    prev_rows, here_rows, next_rows = products(lc, pc_side, po, a_blocks, from_left, p_blocks, from_right)
    from_right_p = shifted(prev_rows, LINE, -1)
    from_left_p = shifted(next_rows, LINE, 1)
    span = NC * B
    combined = jnp.pad(here_rows, ((0, 0), (span, span)))
    combined = combined + jnp.pad(from_right_p, ((0, 0), (2 * span, 0)))
    combined = combined + jnp.pad(from_left_p, ((0, 0), (0, 2 * span)))
    rows_here = combined.astype(jnp.bfloat16)[None]
    group = lax.axis_index("grp")
    joined = rows_here
    for section_bit in range(lax.axis_size("grp").bit_length() - 1):
        partner = partner_2(joined, "grp", section_bit)
        is_upper = group // 2**section_bit % 2 == 1
        joined = jnp.where(
            is_upper,
            jnp.concatenate([partner, joined], axis=0),
            jnp.concatenate([joined, partner], axis=0),
        )
    return joined


def solution(mesh):
    placed = (P(LINE, None),) * 4
    return jax.shard_map(
        local, mesh=mesh, in_specs=placed, out_specs=P(None, "dev", None), check_vma=False
    )
```

```python
import jax
import jax.numpy as jnp
from jax import lax
from jax.experimental import pallas as pl
from jax.experimental.pallas import tpu as pltpu
from jax.sharding import PartitionSpec as P

B = 64
KA = 12
KP = 4
NC = 2
RB = 8
LINE = ("grp", "dev")
HALF = 128


def shifted(x, axis, by):
    peers = lax.axis_size(axis)
    pairs = [(i, i + by) for i in range(peers) if 0 <= i + by < peers]
    return lax.ppermute(x, axis, pairs)


def partner_2(x, axis, bit):
    return lax.ppermute(x, axis, [(i, i ^ 1 << bit) for i in range(lax.axis_size(axis))])


def chunk(j):
    return pl.ds(pl.multiple_of(j * HALF, HALF), HALF)


def rows_at(r):
    return pl.ds(pl.multiple_of(r * B, B), B)


def spread_rows(ps_ref, base, src_ref, pc_ref, pc_base, side):
    for r in range(RB):
        blk = src_ref[r * B : (r + 1) * B, :].astype(jnp.float32)
        halves = [blk[:, 0:HALF], blk[:, HALF : 2 * HALF]]
        swapped = [pltpu.roll(h, B, 1) for h in halves]
        rows = slice((base + r) * B, (base + r + 1) * B)
        for l in range(KP):
            j = pc_ref[pc_base + r, l]
            h = j % 2
            val = jnp.where(h == l % 2, halves[l // 2], swapped[l // 2])
            cols = chunk(j // 2)
            cur = ps_ref[rows, cols].astype(jnp.float32)
            ps_ref[rows, cols] = jnp.where(side == h, val, cur).astype(ps_ref.dtype)


def own_kernel(po_ref, pm_ref, pso_ref, st_ref):
    side = lax.broadcasted_iota(jnp.int32, (B, HALF), 1) // B
    pso_ref[...] = jnp.zeros(pso_ref.shape, pso_ref.dtype)
    spread_rows(pso_ref, 0, pm_ref, po_ref, 0, side)
    pt = pm_ref[...].astype(jnp.float32).T
    st_ref[...] = jnp.zeros(st_ref.shape, st_ref.dtype)
    for i in range(RB):
        cols = slice((i // 2) * HALF, (i // 2 + 1) * HALF)
        for l in range(KP):
            dest = rows_at(po_ref[RB + i, l])
            cur = st_ref[dest, cols].astype(jnp.float32)
            st_ref[dest, cols] = jnp.where(side == i % 2, pt[l * B : (l + 1) * B, cols], cur).astype(st_ref.dtype)


def product_kernel(
    lc_ref, pc_ref, a_ref, pl_ref, pr_ref, pso_ref, st_ref, prev_ref, here_ref, next_ref, ps_ref, panel_ref, ap_ref
):
    side = lax.broadcasted_iota(jnp.int32, (B, HALF), 1) // B
    near = RB * B
    ps_ref[0:near, :] = jnp.zeros((near, ps_ref.shape[1]), ps_ref.dtype)
    ps_ref[2 * near : 3 * near, :] = jnp.zeros((near, ps_ref.shape[1]), ps_ref.dtype)
    ps_ref[near : 2 * near, :] = pso_ref[...]
    spread_rows(ps_ref, 0, pl_ref, pc_ref, 0, side)
    spread_rows(ps_ref, 2 * RB, pr_ref, pc_ref, RB, side)
    for i in range(RB):
        for k in range(KA):
            panel_ref[k * B : (k + 1) * B, :] = ps_ref[rows_at(lc_ref[i, k]), :]
        ap = jnp.dot(a_ref[i * B : (i + 1) * B, :], panel_ref[...], preferred_element_type=jnp.float32)
        ap_ref[i * B : (i + 1) * B, :] = ap.astype(ap_ref.dtype)
    span = NC * B
    for o, out_ref in enumerate((prev_ref, here_ref, next_ref)):
        out_ref[...] = jnp.dot(
            st_ref[o * span : (o + 1) * span, :], ap_ref[...], preferred_element_type=jnp.float32
        )


def products(lc, pc_side, po, a_blocks, left, own, right):
    smem = pl.BlockSpec(memory_space=pltpu.SMEM)
    vmem = pl.BlockSpec(memory_space=pltpu.VMEM)
    window = 5 * NC * B
    pso, st = pl.pallas_call(
        own_kernel,
        out_shape=[
            jax.ShapeDtypeStruct((RB * B, window), jnp.bfloat16),
            jax.ShapeDtypeStruct((3 * NC * B, RB * B), jnp.bfloat16),
        ],
        in_specs=[smem, vmem],
        out_specs=[vmem] * 2,
    )(po, own)
    return pl.pallas_call(
        product_kernel,
        out_shape=[jax.ShapeDtypeStruct((NC * B, window), jnp.float32)] * 3,
        in_specs=[smem] * 2 + [vmem] * 5,
        out_specs=[vmem] * 3,
        scratch_shapes=[
            pltpu.VMEM((3 * RB * B, window), jnp.bfloat16),
            pltpu.VMEM((KA * B, window), jnp.bfloat16),
            pltpu.VMEM((RB * B, window), jnp.bfloat16),
        ],
        cost_estimate=pl.CostEstimate(
            flops=2 * RB * B * KA * B * window + 2 * 3 * NC * B * RB * B * window,
            bytes_accessed=4 * 1024 * 1024,
            transcendentals=0,
        ),
    )(lc, pc_side, a_blocks, left, right, pso, st)


def local(a_blocks, a_cols, p_blocks, p_cols):
    q = lax.axis_index(LINE)
    rel = p_cols - (q - 1) * NC
    tag = jnp.zeros((16, KP * B), jnp.bfloat16).at[:RB, :KP].set(rel.astype(jnp.bfloat16))
    payload = jnp.concatenate([p_blocks, tag], axis=0)
    from_left = shifted(payload, LINE, 1)
    from_right = shifted(payload, LINE, -1)

    def cols(x, shift):
        return x[RB * B : RB * B + RB, :KP].astype(jnp.int32) + shift

    pc_side = jnp.concatenate([cols(from_left, 0), cols(from_right, 2 * NC)], axis=0)
    po = jnp.concatenate([rel + NC, rel], axis=0)
    lc = a_cols - (q - 1) * RB
    prev_rows, here_rows, next_rows = products(lc, pc_side, po, a_blocks, from_left, p_blocks, from_right)
    from_right_p = shifted(prev_rows, LINE, -1)
    from_left_p = shifted(next_rows, LINE, 1)
    span = NC * B
    combined = jnp.pad(here_rows, ((0, 0), (span, span)))
    combined = combined + jnp.pad(from_right_p, ((0, 0), (2 * span, 0)))
    combined = combined + jnp.pad(from_left_p, ((0, 0), (0, 2 * span)))
    rows_here = combined.astype(jnp.bfloat16)[None]
    group = lax.axis_index("grp")
    if lax.axis_size("grp") == 2:
        partner = partner_2(rows_here, "grp", 0)
        joined = jnp.concatenate([rows_here, rows_here], axis=0)
        return lax.dynamic_update_slice_in_dim(joined, partner, 1 - group, axis=0)
    joined = rows_here
    for section_bit in range(lax.axis_size("grp").bit_length() - 1):
        partner = partner_2(joined, "grp", section_bit)
        is_upper = group // 2**section_bit % 2 == 1
        joined = jnp.where(
            is_upper,
            jnp.concatenate([partner, joined], axis=0),
            jnp.concatenate([joined, partner], axis=0),
        )
    return joined


def solution(mesh):
    placed = (P(LINE, None),) * 4
    return jax.shard_map(
        local, mesh=mesh, in_specs=placed, out_specs=P(None, "dev", None), check_vma=False
    )
```

```python
import jax
import jax.numpy as jnp
from jax import lax
from jax.experimental import pallas as pl
from jax.experimental.pallas import tpu as pltpu
from jax.sharding import PartitionSpec as P

B = 64
KA = 12
KP = 4
NC = 2
RB = 8
LINE = ("grp", "dev")
HALF = 128


def shifted(x, axis, by):
    peers = lax.axis_size(axis)
    pairs = [(i, i + by) for i in range(peers) if 0 <= i + by < peers]
    return lax.ppermute(x, axis, pairs)


def inside(x, by):
    n_dev, n = lax.axis_size("dev"), lax.axis_size(LINE)
    pairs = [(i, i + by) for i in range(n) if 0 <= i + by < n and i // n_dev == (i + by) // n_dev]
    return lax.ppermute(x, LINE, pairs)


def across(x):
    n_dev, n = lax.axis_size("dev"), lax.axis_size(LINE)
    pairs = []
    for b in range(n_dev, n, n_dev):
        pairs += [(b - 1, b), (b, b - 1)]
    return lax.ppermute(x, LINE, pairs)


def partner_2(x, axis, bit):
    return lax.ppermute(x, axis, [(i, i ^ 1 << bit) for i in range(lax.axis_size(axis))])


def chunk(j):
    return pl.ds(pl.multiple_of(j * HALF, HALF), HALF)


def rows_at(r):
    return pl.ds(pl.multiple_of(r * B, B), B)


def spread_rows(ps_ref, base, src_ref, pc_ref, pc_base, side, edge=None):
    for r in range(RB):
        blk = src_ref[r * B : (r + 1) * B, :]
        if edge is not None:
            edge_ref, use_edge = edge
            blk = jnp.where(use_edge, edge_ref[r * B : (r + 1) * B, :], blk)
        blk = blk.astype(jnp.float32)
        halves = [blk[:, 0:HALF], blk[:, HALF : 2 * HALF]]
        swapped = [pltpu.roll(h, B, 1) for h in halves]
        rows = slice((base + r) * B, (base + r + 1) * B)
        for l in range(KP):
            j = pc_ref[pc_base + r, l]
            h = j % 2
            val = jnp.where(h == l % 2, halves[l // 2], swapped[l // 2])
            cols = chunk(j // 2)
            cur = ps_ref[rows, cols].astype(jnp.float32)
            ps_ref[rows, cols] = jnp.where(side == h, val, cur).astype(ps_ref.dtype)


def own_kernel(po_ref, pm_ref, pso_ref, st_ref):
    side = lax.broadcasted_iota(jnp.int32, (B, HALF), 1) // B
    pso_ref[...] = jnp.zeros(pso_ref.shape, pso_ref.dtype)
    spread_rows(pso_ref, 0, pm_ref, po_ref, 0, side)
    pt = pm_ref[...].astype(jnp.float32).T
    st_ref[...] = jnp.zeros(st_ref.shape, st_ref.dtype)
    for i in range(RB):
        cols = slice((i // 2) * HALF, (i // 2 + 1) * HALF)
        for l in range(KP):
            dest = rows_at(po_ref[RB + i, l])
            cur = st_ref[dest, cols].astype(jnp.float32)
            st_ref[dest, cols] = jnp.where(side == i % 2, pt[l * B : (l + 1) * B, cols], cur).astype(st_ref.dtype)


def product_kernel(
    flag_ref, lc_ref, pc_ref, a_ref, pl_ref, pr_ref, pe_ref, pso_ref, st_ref,
    prev_ref, here_ref, next_ref, edge_ref, ps_ref, panel_ref, ap_ref,
):
    first = flag_ref[0] == 1
    last = flag_ref[1] == 1
    side = lax.broadcasted_iota(jnp.int32, (B, HALF), 1) // B
    near = RB * B
    ps_ref[0:near, :] = jnp.zeros((near, ps_ref.shape[1]), ps_ref.dtype)
    ps_ref[2 * near : 3 * near, :] = jnp.zeros((near, ps_ref.shape[1]), ps_ref.dtype)
    ps_ref[near : 2 * near, :] = pso_ref[...]
    spread_rows(ps_ref, 0, pl_ref, pc_ref, 0, side, (pe_ref, first))
    spread_rows(ps_ref, 2 * RB, pr_ref, pc_ref, RB, side, (pe_ref, last))
    for i in range(RB):
        for k in range(KA):
            panel_ref[k * B : (k + 1) * B, :] = ps_ref[rows_at(lc_ref[i, k]), :]
        ap = jnp.dot(a_ref[i * B : (i + 1) * B, :], panel_ref[...], preferred_element_type=jnp.float32)
        ap_ref[i * B : (i + 1) * B, :] = ap.astype(ap_ref.dtype)
    span = NC * B
    res = jnp.dot(st_ref[...], ap_ref[...], preferred_element_type=jnp.float32)
    prev_ref[...] = res[0:span]
    here_ref[...] = res[span : 2 * span]
    next_ref[...] = res[2 * span : 3 * span]
    edge_ref[...] = jnp.where(last, res[2 * span : 3 * span], res[0:span])


def products(flags, lc, pc_side, po, a_blocks, left, own, right, edge):
    smem = pl.BlockSpec(memory_space=pltpu.SMEM)
    vmem = pl.BlockSpec(memory_space=pltpu.VMEM)
    window = 5 * NC * B
    pso, st = pl.pallas_call(
        own_kernel,
        out_shape=[
            jax.ShapeDtypeStruct((RB * B, window), jnp.bfloat16),
            jax.ShapeDtypeStruct((3 * NC * B, RB * B), jnp.bfloat16),
        ],
        in_specs=[smem, vmem],
        out_specs=[vmem] * 2,
    )(po, own)
    return pl.pallas_call(
        product_kernel,
        out_shape=[jax.ShapeDtypeStruct((NC * B, window), jnp.float32)] * 4,
        in_specs=[smem] * 3 + [vmem] * 6,
        out_specs=[vmem] * 4,
        scratch_shapes=[
            pltpu.VMEM((3 * RB * B, window), jnp.bfloat16),
            pltpu.VMEM((KA * B, window), jnp.bfloat16),
            pltpu.VMEM((RB * B, window), jnp.bfloat16),
        ],
        cost_estimate=pl.CostEstimate(
            flops=2 * RB * B * KA * B * window + 2 * 3 * NC * B * RB * B * window,
            bytes_accessed=4 * 1024 * 1024,
            transcendentals=0,
        ),
    )(flags, lc, pc_side, a_blocks, left, right, edge, pso, st)


def local(a_blocks, a_cols, p_blocks, p_cols):
    q = lax.axis_index(LINE)
    rel = p_cols - (q - 1) * NC
    tag = jnp.zeros((16, KP * B), jnp.bfloat16).at[:RB, :KP].set(rel.astype(jnp.bfloat16))
    payload = jnp.concatenate([p_blocks, tag], axis=0)
    n_dev, n = lax.axis_size("dev"), lax.axis_size(LINE)
    d, g = lax.axis_index("dev"), lax.axis_index("grp")
    first = (d == 0) & (q > 0)
    last = (d == n_dev - 1) & (q < n - 1)
    flags = jnp.stack([first, last]).astype(jnp.int32)
    from_left = inside(payload, 1)
    from_right = inside(payload, -1)
    edge = across(payload)

    def cols(x, shift):
        return x[RB * B : RB * B + RB, :KP].astype(jnp.int32) + shift

    pc_side = jnp.concatenate(
        [
            jnp.where(first, cols(edge, 0), cols(from_left, 0)),
            jnp.where(last, cols(edge, 2 * NC), cols(from_right, 2 * NC)),
        ],
        axis=0,
    )
    po = jnp.concatenate([rel + NC, rel], axis=0)
    lc = a_cols - (q - 1) * RB
    prev_rows, here_rows, next_rows, edge_rows = products(
        flags, lc, pc_side, po, a_blocks, from_left, p_blocks, from_right, edge
    )
    edge_p = across(edge_rows)
    from_right_p = jnp.where(last, edge_p, inside(prev_rows, -1))
    from_left_p = jnp.where(first, edge_p, inside(next_rows, 1))
    span = NC * B
    combined = jnp.pad(here_rows, ((0, 0), (span, span)))
    combined = combined + jnp.pad(from_right_p, ((0, 0), (2 * span, 0)))
    combined = combined + jnp.pad(from_left_p, ((0, 0), (0, 2 * span)))
    rows_here = combined.astype(jnp.bfloat16)[None]
    group = lax.axis_index("grp")
    if lax.axis_size("grp") == 2:
        partner = partner_2(rows_here, "grp", 0)
        joined = jnp.concatenate([rows_here, rows_here], axis=0)
        return lax.dynamic_update_slice_in_dim(joined, partner, 1 - group, axis=0)
    joined = rows_here
    for section_bit in range(lax.axis_size("grp").bit_length() - 1):
        partner = partner_2(joined, "grp", section_bit)
        is_upper = group // 2**section_bit % 2 == 1
        joined = jnp.where(
            is_upper,
            jnp.concatenate([partner, joined], axis=0),
            jnp.concatenate([joined, partner], axis=0),
        )
    return joined


def solution(mesh):
    placed = (P(LINE, None),) * 4
    return jax.shard_map(
        local, mesh=mesh, in_specs=placed, out_specs=P(None, "dev", None), check_vma=False
    )
```

```python
import jax
import jax.numpy as jnp
from jax import lax
from jax.experimental import pallas as pl
from jax.experimental.pallas import tpu as pltpu
from jax.sharding import PartitionSpec as P


B = 64
KA = 12
KP = 4
NC = 2
RB = 8
LINE = ("grp", "dev")
HALF = 128


def inside(x, by):
    n_dev, n = lax.axis_size("dev"), lax.axis_size(LINE)
    pairs = [(i, i + by) for i in range(n) if 0 <= i + by < n and i // n_dev == (i + by) // n_dev]
    return lax.ppermute(x, LINE, pairs)


def across(x):
    n_dev, n = lax.axis_size("dev"), lax.axis_size(LINE)
    pairs = []
    for b in range(n_dev, n, n_dev):
        pairs += [(b - 1, b), (b, b - 1)]
    return lax.ppermute(x, LINE, pairs)


def partner_2(x, axis, bit):
    return lax.ppermute(x, axis, [(i, i ^ 1 << bit) for i in range(lax.axis_size(axis))])


def chunk(j):
    return pl.ds(pl.multiple_of(j * HALF, HALF), HALF)


def rows_at(r):
    return pl.ds(pl.multiple_of(r * B, B), B)


def spread_rows(ps_ref, base, src_ref, pc_ref, pc_base, side, edge=None):
    for r in range(RB):
        blk = src_ref[r * B : (r + 1) * B, :]
        if edge is not None:
            edge_ref, use_edge = edge
            blk = jnp.where(use_edge, edge_ref[r * B : (r + 1) * B, :], blk)
        blk = blk.astype(jnp.float32)
        halves = [blk[:, 0:HALF], blk[:, HALF : 2 * HALF]]
        swapped = [pltpu.roll(h, B, 1) for h in halves]
        rows = slice((base + r) * B, (base + r + 1) * B)
        for l in range(KP):
            j = pc_ref[pc_base + r, l]
            h = j % 2
            val = jnp.where(h == l % 2, halves[l // 2], swapped[l // 2])
            cols = chunk(j // 2)
            cur = ps_ref[rows, cols].astype(jnp.float32)
            ps_ref[rows, cols] = jnp.where(side == h, val, cur).astype(ps_ref.dtype)


def own_kernel(po_ref, pm_ref, pso_ref, st_ref):
    side = lax.broadcasted_iota(jnp.int32, (B, HALF), 1) // B
    pso_ref[...] = jnp.zeros(pso_ref.shape, pso_ref.dtype)
    spread_rows(pso_ref, 0, pm_ref, po_ref, 0, side)
    pt = pm_ref[...].astype(jnp.float32).T
    st_ref[...] = jnp.zeros(st_ref.shape, st_ref.dtype)
    for i in range(RB):
        cols = slice((i // 2) * HALF, (i // 2 + 1) * HALF)
        for l in range(KP):
            dest = rows_at(po_ref[RB + i, l])
            cur = st_ref[dest, cols].astype(jnp.float32)
            st_ref[dest, cols] = jnp.where(side == i % 2, pt[l * B : (l + 1) * B, cols], cur).astype(st_ref.dtype)


def product_kernel(
    flag_ref, lc_ref, pc_ref, a_ref, pl_ref, pr_ref, pe_ref, pso_ref, st_ref,
    prev_ref, here_ref, next_ref, edge_ref, ps_ref, panel_ref, ap_ref,
):
    first = flag_ref[0] == 1
    last = flag_ref[1] == 1
    side = lax.broadcasted_iota(jnp.int32, (B, HALF), 1) // B
    near = RB * B
    ps_ref[0:near, :] = jnp.zeros((near, ps_ref.shape[1]), ps_ref.dtype)
    ps_ref[2 * near : 3 * near, :] = jnp.zeros((near, ps_ref.shape[1]), ps_ref.dtype)
    ps_ref[near : 2 * near, :] = pso_ref[...]
    spread_rows(ps_ref, 0, pl_ref, pc_ref, 0, side, (pe_ref, first))
    spread_rows(ps_ref, 2 * RB, pr_ref, pc_ref, RB, side, (pe_ref, last))
    for i in range(RB):
        for k in range(KA):
            panel_ref[k * B : (k + 1) * B, :] = ps_ref[rows_at(lc_ref[i, k]), :]
        ap = jnp.dot(a_ref[i * B : (i + 1) * B, :], panel_ref[...], preferred_element_type=jnp.float32)
        ap_ref[i * B : (i + 1) * B, :] = ap.astype(ap_ref.dtype)
    span = NC * B
    res = jnp.dot(st_ref[...], ap_ref[...], preferred_element_type=jnp.float32)
    prev_ref[...] = res[0:span]
    here_ref[...] = res[span : 2 * span]
    next_ref[...] = res[2 * span : 3 * span]
    edge_ref[...] = jnp.where(last, res[2 * span : 3 * span], res[0:span])


def products(flags, lc, pc_side, po, a_blocks, left, own, right, edge):
    smem = pl.BlockSpec(memory_space=pltpu.SMEM)
    vmem = pl.BlockSpec(memory_space=pltpu.VMEM)
    window = 5 * NC * B
    pso, st = pl.pallas_call(
        own_kernel,
        out_shape=[
            jax.ShapeDtypeStruct((RB * B, window), jnp.bfloat16),
            jax.ShapeDtypeStruct((3 * NC * B, RB * B), jnp.bfloat16),
        ],
        in_specs=[smem, vmem],
        out_specs=[vmem] * 2,
    )(po, own)
    return pl.pallas_call(
        product_kernel,
        out_shape=[jax.ShapeDtypeStruct((NC * B, window), jnp.float32)] * 4,
        in_specs=[smem] * 3 + [vmem] * 6,
        out_specs=[vmem] * 4,
        scratch_shapes=[
            pltpu.VMEM((3 * RB * B, window), jnp.bfloat16),
            pltpu.VMEM((KA * B, window), jnp.bfloat16),
            pltpu.VMEM((RB * B, window), jnp.bfloat16),
        ],
        cost_estimate=pl.CostEstimate(
            flops=2 * RB * B * KA * B * window + 2 * 3 * NC * B * RB * B * window,
            bytes_accessed=4 * 1024 * 1024,
            transcendentals=0,
        ),
    )(flags, lc, pc_side, a_blocks, left, right, edge, pso, st)


def local(a_blocks, a_cols, p_blocks, p_cols):
    q = lax.axis_index(LINE)
    rel = p_cols - (q - 1) * NC
    tag = jnp.zeros((16, KP * B), jnp.bfloat16).at[:RB, :KP].set(rel.astype(jnp.bfloat16))
    payload = jnp.concatenate([p_blocks, tag], axis=0)
    n_dev, n = lax.axis_size("dev"), lax.axis_size(LINE)
    d = lax.axis_index("dev")
    first = (d == 0) & (q > 0)
    last = (d == n_dev - 1) & (q < n - 1)
    flags = jnp.stack([first, last]).astype(jnp.int32)
    edge = across(payload)
    from_left = inside(payload, 1)
    from_right = inside(payload, -1)

    def cols(x, shift):
        return x[RB * B : RB * B + RB, :KP].astype(jnp.int32) + shift

    pc_side = jnp.concatenate(
        [
            jnp.where(first, cols(edge, 0), cols(from_left, 0)),
            jnp.where(last, cols(edge, 2 * NC), cols(from_right, 2 * NC)),
        ],
        axis=0,
    )
    po = jnp.concatenate([rel + NC, rel], axis=0)
    lc = a_cols - (q - 1) * RB
    prev_rows, here_rows, next_rows, edge_rows = products(
        flags, lc, pc_side, po, a_blocks, from_left, p_blocks, from_right, edge
    )
    edge_p = across(edge_rows)
    from_right_p = jnp.where(last, edge_p, inside(prev_rows, -1))
    from_left_p = jnp.where(first, edge_p, inside(next_rows, 1))
    span = NC * B
    combined = jnp.pad(here_rows, ((0, 0), (span, span)))
    combined = combined + jnp.pad(from_right_p, ((0, 0), (2 * span, 0)))
    combined = combined + jnp.pad(from_left_p, ((0, 0), (0, 2 * span)))
    rows_here = combined.astype(jnp.bfloat16)[None]
    group = lax.axis_index("grp")
    if lax.axis_size("grp") == 2:
        partner = partner_2(rows_here, "grp", 0)
        joined = jnp.concatenate([rows_here, rows_here], axis=0)
        return lax.dynamic_update_slice_in_dim(joined, partner, 1 - group, axis=0)
    joined = rows_here
    for section_bit in range(lax.axis_size("grp").bit_length() - 1):
        partner = partner_2(joined, "grp", section_bit)
        is_upper = group // 2**section_bit % 2 == 1
        joined = jnp.where(
            is_upper,
            jnp.concatenate([partner, joined], axis=0),
            jnp.concatenate([joined, partner], axis=0),
        )
    return joined


def solution(mesh):
    placed = (P(LINE, None),) * 4
    return jax.shard_map(
        local, mesh=mesh, in_specs=placed, out_specs=P(None, "dev", None), check_vma=False
    )
```

```python
import functools

import jax
import jax.numpy as jnp
from jax import lax
from jax.experimental import pallas as pl
from jax.experimental.pallas import tpu as pltpu
from jax.sharding import PartitionSpec as P


B = 64
KA = 12
KP = 4
NC = 2
RB = 8
LINE = ("grp", "dev")
HALF = 128


def inside(x, by):
    n_dev, n = lax.axis_size("dev"), lax.axis_size(LINE)
    pairs = [(i, i + by) for i in range(n) if 0 <= i + by < n and i // n_dev == (i + by) // n_dev]
    return lax.ppermute(x, LINE, pairs)


def across(x):
    n_dev, n = lax.axis_size("dev"), lax.axis_size(LINE)
    pairs = []
    for b in range(n_dev, n, n_dev):
        pairs += [(b - 1, b), (b, b - 1)]
    return lax.ppermute(x, LINE, pairs)


def partner_2(x, axis, bit):
    return lax.ppermute(x, axis, [(i, i ^ 1 << bit) for i in range(lax.axis_size(axis))])


def chunk(j):
    return pl.ds(pl.multiple_of(j * HALF, HALF), HALF)


def rows_at(r):
    return pl.ds(pl.multiple_of(r * B, B), B)


def spread_rows(ps_ref, base, src_ref, pc_ref, pc_base, side, edge=None, shift=0):
    for r in range(RB):
        blk = src_ref[r * B : (r + 1) * B, :]
        if edge is not None:
            edge_ref, use_edge = edge
            blk = jnp.where(use_edge, edge_ref[r * B : (r + 1) * B, :], blk)
        blk = blk.astype(jnp.float32)
        halves = [blk[:, 0:HALF], blk[:, HALF : 2 * HALF]]
        swapped = [pltpu.roll(h, B, 1) for h in halves]
        rows = slice((base + r) * B, (base + r + 1) * B)
        for l in range(KP):
            j = pc_ref[pc_base + r, l] + shift
            h = j % 2
            val = jnp.where(h == l % 2, halves[l // 2], swapped[l // 2])
            cols = chunk(j // 2)
            cur = ps_ref[rows, cols].astype(jnp.float32)
            ps_ref[rows, cols] = jnp.where(side == h, val, cur).astype(ps_ref.dtype)


def line_index(n_dev):
    return lax.axis_index("grp") * n_dev + lax.axis_index("dev")


def product_kernel(
    n_dev, n, acol_ref, pcol_ref, pc_ref, a_ref, pl_ref, pm_ref, pr_ref, pe_ref,
    prev_ref, here_ref, next_ref, edge_ref, ps_ref, panel_ref, ap_ref, st_ref,
):
    q = line_index(n_dev)
    d = lax.axis_index("dev")
    first = (d == 0) & (q > 0)
    last = (d == n_dev - 1) & (q < n - 1)
    side = lax.broadcasted_iota(jnp.int32, (B, HALF), 1) // B
    ps_ref[...] = jnp.zeros(ps_ref.shape, ps_ref.dtype)
    spread_rows(ps_ref, 0, pl_ref, pc_ref, 0, side, (pe_ref, first))
    spread_rows(ps_ref, RB, pm_ref, pcol_ref, 0, side, shift=-(q - 2) * NC)
    spread_rows(ps_ref, 2 * RB, pr_ref, pc_ref, RB, side, (pe_ref, last))
    for i in range(RB):
        for k in range(KA):
            panel_ref[k * B : (k + 1) * B, :] = ps_ref[rows_at(acol_ref[i, k] - (q - 1) * RB), :]
        ap = jnp.dot(a_ref[i * B : (i + 1) * B, :], panel_ref[...], preferred_element_type=jnp.float32)
        ap_ref[i * B : (i + 1) * B, :] = ap.astype(ap_ref.dtype)
    pt = pm_ref[...].astype(jnp.float32).T
    st_ref[...] = jnp.zeros(st_ref.shape, st_ref.dtype)
    for i in range(RB):
        cols = slice((i // 2) * HALF, (i // 2 + 1) * HALF)
        for l in range(KP):
            dest = rows_at(pcol_ref[i, l] - (q - 1) * NC)
            cur = st_ref[dest, cols]
            st_ref[dest, cols] = jnp.where(side == i % 2, pt[l * B : (l + 1) * B, cols], cur)
    span = NC * B
    res = jnp.dot(st_ref[...].astype(jnp.bfloat16), ap_ref[...], preferred_element_type=jnp.float32)
    prev_ref[...] = res[0:span]
    here_ref[...] = res[span : 2 * span]
    next_ref[...] = res[2 * span : 3 * span]
    edge_ref[...] = jnp.where(last, res[2 * span : 3 * span], res[0:span])


def products(a_cols, pc_side, p_cols, a_blocks, left, own, right, edge):
    n_dev, n = lax.axis_size("dev"), lax.axis_size(LINE)
    smem = pl.BlockSpec(memory_space=pltpu.SMEM)
    vmem = pl.BlockSpec(memory_space=pltpu.VMEM)
    window = 5 * NC * B
    return pl.pallas_call(
        functools.partial(product_kernel, n_dev, n),
        out_shape=[jax.ShapeDtypeStruct((NC * B, window), jnp.float32)] * 4,
        in_specs=[smem] * 3 + [vmem] * 5,
        out_specs=[vmem] * 4,
        scratch_shapes=[
            pltpu.VMEM((3 * RB * B, window), jnp.bfloat16),
            pltpu.VMEM((KA * B, window), jnp.bfloat16),
            pltpu.VMEM((RB * B, window), jnp.bfloat16),
            pltpu.VMEM((3 * NC * B, RB * B), jnp.float32),
        ],
        cost_estimate=pl.CostEstimate(
            flops=2 * RB * B * KA * B * window + 2 * 3 * NC * B * RB * B * window,
            bytes_accessed=4 * 1024 * 1024,
            transcendentals=0,
        ),
    )(a_cols, p_cols, pc_side, a_blocks, left, own, right, edge)


def local(a_blocks, a_cols, p_blocks, p_cols):
    q = lax.axis_index(LINE)
    rel = p_cols - (q - 1) * NC
    tag = jnp.zeros((16, KP * B), jnp.bfloat16).at[:RB, :KP].set(rel.astype(jnp.bfloat16))
    payload = jnp.concatenate([p_blocks, tag], axis=0)
    n_dev, n = lax.axis_size("dev"), lax.axis_size(LINE)
    d = lax.axis_index("dev")
    first = (d == 0) & (q > 0)
    last = (d == n_dev - 1) & (q < n - 1)
    edge = across(payload)
    from_left = inside(payload, 1)
    from_right = inside(payload, -1)

    def cols(x, shift):
        return x[RB * B : RB * B + RB, :KP].astype(jnp.int32) + shift

    pc_side = jnp.concatenate(
        [
            jnp.where(first, cols(edge, 0), cols(from_left, 0)),
            jnp.where(last, cols(edge, 2 * NC), cols(from_right, 2 * NC)),
        ],
        axis=0,
    )
    prev_rows, here_rows, next_rows, edge_rows = products(
        a_cols, pc_side, p_cols, a_blocks, from_left, p_blocks, from_right, edge
    )
    edge_p = across(edge_rows)
    from_right_p = jnp.where(last, edge_p, inside(prev_rows, -1))
    from_left_p = jnp.where(first, edge_p, inside(next_rows, 1))
    span = NC * B
    combined = jnp.pad(here_rows, ((0, 0), (span, span)))
    combined = combined + jnp.pad(from_right_p, ((0, 0), (2 * span, 0)))
    combined = combined + jnp.pad(from_left_p, ((0, 0), (0, 2 * span)))
    rows_here = combined.astype(jnp.bfloat16)[None]
    group = lax.axis_index("grp")
    if lax.axis_size("grp") == 2:
        partner = partner_2(rows_here, "grp", 0)
        joined = jnp.concatenate([rows_here, rows_here], axis=0)
        return lax.dynamic_update_slice_in_dim(joined, partner, 1 - group, axis=0)
    joined = rows_here
    for section_bit in range(lax.axis_size("grp").bit_length() - 1):
        partner = partner_2(joined, "grp", section_bit)
        is_upper = group // 2**section_bit % 2 == 1
        joined = jnp.where(
            is_upper,
            jnp.concatenate([partner, joined], axis=0),
            jnp.concatenate([joined, partner], axis=0),
        )
    return joined


def solution(mesh):
    placed = (P(LINE, None),) * 4
    return jax.shard_map(
        local, mesh=mesh, in_specs=placed, out_specs=P(None, "dev", None), check_vma=False
    )
```
